128 devices in a mesh: head: 4 (over x), ctx: 8 (over y, z_hi), inner: 4 (over z_lo, core).
Axes of the slice: x: 4, y: 4, z: 4 (z_hi: 2, z_lo: 2; z = z_hi * 2 + z_lo), core: 2. Of those that a mesh axis runs over, the one named last changes fastest.
Arguments:
- query_rows: bfloat16 [16384, 48, 128], P(('head', 'ctx', 'inner')), may hold values from -6 to 6
- key_rows: bfloat16 [16384, 48, 128], P(('head', 'ctx', 'inner')), may hold values from -6 to 6
- value_rows: bfloat16 [16384, 48, 128], P(('head', 'ctx', 'inner')), may hold values from -6 to 6
- grad_rows: bfloat16 [16384, 48, 128], P(('head', 'ctx', 'inner')), may hold values from -6 to 6
Outputs:
- grad_query: bfloat16 [16384, 48, 128], P(('head', 'ctx', 'inner'))
- grad_key: bfloat16 [16384, 48, 128], P(('head', 'ctx', 'inner'))
- grad_value: bfloat16 [16384, 48, 128], P(('head', 'ctx', 'inner'))
The draws below stay inside these ranges and needn't reach their ends.
All inputs are finite; a program needn't handle non-finite values.
Results may differ from the reference program's by a relative error of at most 0.012.
The reference program's roundings to bfloat16 on the way count: a program that leaves them out, or rounds other values in their place, can miss the bound.
Values may be sent and summed in bfloat16 or wider, within the bound.
No kernel may reach another device: no remote copies, remote signals or barrier semaphores. Data moves between devices by JAX's collectives and lax.ppermute only.
A program may use at most 128 MiB of HBM per device.

```python
import jax
import jax.numpy as jnp
from jax import lax

HEADS = 48
HD = 128
TOK_DEV = 128
SEQ = 16384
SHARDS = 32
BLOCK = 256


def draw_query_rows(key, part):
    base_key = jax.random.fold_in(key, 1)
    drawn = jax.random.truncated_normal(base_key, -6.0, 6.0, (SEQ, HEADS, HD), jnp.float32)
    return drawn.astype(jnp.bfloat16)


def draw_key_rows(key, part):
    base_key = jax.random.fold_in(key, 2)
    drawn = jax.random.truncated_normal(base_key, -6.0, 6.0, (SEQ, HEADS, HD), jnp.float32)
    return drawn.astype(jnp.bfloat16)


def block_levels(rng, shape, pieces, smallest, high):
    level, own = 1.0, jax.random.fold_in(rng, 6)
    for axis_at, blocks in pieces:
        steps = jnp.exp(jax.random.uniform(jax.random.fold_in(own, axis_at), (blocks,), jnp.float32, smallest / len(pieces), high / len(pieces)))
        level = level * jnp.repeat(steps, shape[axis_at] // blocks).reshape([-1 if axis == axis_at else 1 for axis in range(len(shape))])
    return level


def normal_values(own_key, dims, deviation, limit, shards=(), kind=jnp.bfloat16):
    drawn = deviation * jax.random.normal(own_key, dims, jnp.float32)
    if shards:
        drawn = drawn * block_levels(own_key, dims, shards, -0.22, 0.18)
    return jnp.clip(drawn, -limit, limit).astype(kind)


def setup_inputs(seed: int = 0) -> dict:
    keys = jax.random.split(jax.random.key(seed), 5)
    query_rows = draw_query_rows(jax.random.fold_in(keys[4], 71), 0)
    key_rows = draw_key_rows(jax.random.fold_in(keys[4], 71), 0)
    value_rows = normal_values(keys[2], (SEQ, HEADS, HD), 1.0, 6.0, ((0, 128),))
    grad_rows = normal_values(keys[3], (SEQ, HEADS, HD), 1.0, 6.0, ((0, 128),))
    return dict(query_rows=query_rows, key_rows=key_rows, value_rows=value_rows, grad_rows=grad_rows)


def token_positions():
    row_ids = jnp.arange(SEQ, dtype=jnp.int32)
    head_part = row_ids // (TOK_DEV * SHARDS)
    shard_id = (row_ids // TOK_DEV) % SHARDS
    within = head_part * TOK_DEV + row_ids % TOK_DEV
    first_pos = shard_id * BLOCK + within
    second_pos = (2 * SHARDS - 1 - shard_id) * BLOCK + within - BLOCK
    return jnp.where(within < BLOCK, first_pos, second_pos).astype(jnp.int32)


def block_grads(query_block, grad_block, key_prev, value_prev, key_own, value_own, prev_valid):
    score_scale = HD ** -0.5
    query_full = query_block.astype(jnp.float32)
    grad_full = grad_block.astype(jnp.float32)
    key_prev_full = key_prev.astype(jnp.float32)
    value_prev_full = value_prev.astype(jnp.float32)
    key_own_full = key_own.astype(jnp.float32)
    value_own_full = value_own.astype(jnp.float32)
    row_count = query_block.shape[0]
    rows_iota = lax.broadcasted_iota(jnp.int32, (row_count, row_count), 0)
    cols_iota = lax.broadcasted_iota(jnp.int32, (row_count, row_count), 1)
    sees_prev = (cols_iota > rows_iota) & prev_valid
    sees_own = cols_iota <= rows_iota
    scores_prev = jnp.einsum("ihd,jhd->hij", query_full, key_prev_full) * score_scale
    scores_own = jnp.einsum("ihd,jhd->hij", query_full, key_own_full) * score_scale
    row_top = jnp.maximum(jnp.max(jnp.where(sees_prev, scores_prev, -jnp.inf), axis=-1),
                          jnp.max(jnp.where(sees_own, scores_own, -jnp.inf), axis=-1))
    row_total = jnp.sum(jnp.where(sees_prev, jnp.exp(scores_prev - row_top[..., None]), 0.0), axis=-1)
    row_total = row_total + jnp.sum(jnp.where(sees_own, jnp.exp(scores_own - row_top[..., None]), 0.0), axis=-1)
    log_total = row_top + jnp.log(row_total)
    prob_prev = jnp.where(sees_prev, jnp.exp(scores_prev - log_total[..., None]), 0.0)
    prob_own = jnp.where(sees_own, jnp.exp(scores_own - log_total[..., None]), 0.0)
    prob_prev_b = prob_prev.astype(jnp.bfloat16).astype(jnp.float32)
    prob_own_b = prob_own.astype(jnp.bfloat16).astype(jnp.float32)
    attended = jnp.einsum("hij,jhd->ihd", prob_prev_b, value_prev_full) + jnp.einsum("hij,jhd->ihd", prob_own_b, value_own_full)
    row_delta = jnp.sum(grad_full * attended, axis=-1).T
    dprob_prev = jnp.einsum("ihd,jhd->hij", grad_full, value_prev_full)
    dprob_own = jnp.einsum("ihd,jhd->hij", grad_full, value_own_full)
    dscore_prev = (prob_prev * (dprob_prev - row_delta[..., None])).astype(jnp.bfloat16).astype(jnp.float32)
    dscore_own = (prob_own * (dprob_own - row_delta[..., None])).astype(jnp.bfloat16).astype(jnp.float32)
    grad_q = (jnp.einsum("hij,jhd->ihd", dscore_prev, key_prev_full) + jnp.einsum("hij,jhd->ihd", dscore_own, key_own_full)) * score_scale
    grad_k_own = jnp.einsum("hij,ihd->jhd", dscore_own, query_full) * score_scale
    grad_v_own = jnp.einsum("hij,ihd->jhd", prob_own_b, grad_full)
    grad_k_prev = jnp.einsum("hij,ihd->jhd", dscore_prev, query_full) * score_scale
    grad_v_prev = jnp.einsum("hij,ihd->jhd", prob_prev_b, grad_full)
    return grad_q, grad_k_own, grad_v_own, grad_k_prev, grad_v_prev


def reference(query_rows, key_rows, value_rows, grad_rows):
    positions = token_positions()
    seq_order = jnp.zeros((SEQ,), jnp.int32).at[positions].set(jnp.arange(SEQ, dtype=jnp.int32))
    block_total = 2 * SHARDS

    def to_blocks(array):
        return array[seq_order].reshape(block_total, BLOCK, HEADS, HD)

    query_blocks = to_blocks(query_rows)
    key_blocks = to_blocks(key_rows)
    value_blocks = to_blocks(value_rows)
    grad_blocks = to_blocks(grad_rows)
    zero_block = jnp.zeros((1, BLOCK, HEADS, HD), key_rows.dtype)
    key_before = jnp.concatenate([zero_block, key_blocks[:-1]], axis=0)
    value_before = jnp.concatenate([zero_block, value_blocks[:-1]], axis=0)
    prev_flags = jnp.arange(block_total) > 0

    def block_step(carried, inputs):
        query_block, grad_block, key_prev, value_prev, key_own, value_own, prev_valid = inputs
        grad_q, grad_k_own, grad_v_own, grad_k_prev, grad_v_prev = block_grads(
            query_block, grad_block, key_prev, value_prev, key_own, value_own, prev_valid)
        grad_k = grad_k_own + carried[0]
        grad_v = grad_v_own + carried[1]
        return (grad_k_prev, grad_v_prev), (grad_q.astype(jnp.bfloat16), grad_k.astype(jnp.bfloat16), grad_v.astype(jnp.bfloat16))

    start_grads = (jnp.zeros((BLOCK, HEADS, HD), jnp.float32), jnp.zeros((BLOCK, HEADS, HD), jnp.float32))
    inputs = (query_blocks, grad_blocks, key_before, value_before, key_blocks, value_blocks, prev_flags)
    unused, outputs = lax.scan(block_step, start_grads, inputs, reverse=True)
    grad_q_seq = outputs[0].reshape(SEQ, HEADS, HD)
    grad_k_seq = outputs[1].reshape(SEQ, HEADS, HD)
    grad_v_seq = outputs[2].reshape(SEQ, HEADS, HD)
    return grad_q_seq[positions], grad_k_seq[positions], grad_v_seq[positions]
```

```python
import jax
import jax.numpy as jnp
from jax import lax
from jax.sharding import PartitionSpec as P

CHUNKS = 4
ALL_AXES = ("head", "ctx", "inner")


def tile_scores(query_block, key_block, score_scale):
    return (
        jnp.einsum("ihd,jhd->hij", query_block, key_block, preferred_element_type=jnp.float32)
        * score_scale
    )


def tile_sight(row_count, prev_valid):
    rows_iota = lax.broadcasted_iota(jnp.int32, (row_count, row_count), 0)
    cols_iota = lax.broadcasted_iota(jnp.int32, (row_count, row_count), 1)
    return ((cols_iota > rows_iota) & prev_valid, cols_iota <= rows_iota)


def block_side(query_block, grad_block, key_prev, value_prev, key_own, value_own, prev_valid):
    score_scale = query_block.shape[-1] ** (-0.5)
    sees_prev, sees_own = tile_sight(query_block.shape[0], prev_valid)
    scores_prev = tile_scores(query_block, key_prev, score_scale)
    scores_own = tile_scores(query_block, key_own, score_scale)
    row_top = jnp.maximum(
        jnp.max(jnp.where(sees_prev, scores_prev, -jnp.inf), axis=-1),
        jnp.max(jnp.where(sees_own, scores_own, -jnp.inf), axis=-1),
    )
    row_total = jnp.sum(
        jnp.where(sees_prev, jnp.exp(scores_prev - row_top[..., None]), 0.0), axis=-1
    )
    row_total = row_total + jnp.sum(
        jnp.where(sees_own, jnp.exp(scores_own - row_top[..., None]), 0.0), axis=-1
    )
    log_total = row_top + jnp.log(row_total)
    prob_prev = jnp.where(sees_prev, jnp.exp(scores_prev - log_total[..., None]), 0.0)
    prob_own = jnp.where(sees_own, jnp.exp(scores_own - log_total[..., None]), 0.0)
    prob_prev_b = prob_prev.astype(jnp.bfloat16)
    prob_own_b = prob_own.astype(jnp.bfloat16)
    attended = jnp.einsum(
        "hij,jhd->ihd", prob_prev_b, value_prev, preferred_element_type=jnp.float32
    )
    attended = attended + jnp.einsum(
        "hij,jhd->ihd", prob_own_b, value_own, preferred_element_type=jnp.float32
    )
    row_delta = jnp.sum(grad_block.astype(jnp.float32) * attended, axis=-1).T
    dprob_prev = jnp.einsum(
        "ihd,jhd->hij", grad_block, value_prev, preferred_element_type=jnp.float32
    )
    dprob_own = jnp.einsum(
        "ihd,jhd->hij", grad_block, value_own, preferred_element_type=jnp.float32
    )
    dscore_prev = (prob_prev * (dprob_prev - row_delta[..., None])).astype(jnp.bfloat16)
    dscore_own = (prob_own * (dprob_own - row_delta[..., None])).astype(jnp.bfloat16)
    grad_q = jnp.einsum("hij,jhd->ihd", dscore_prev, key_prev, preferred_element_type=jnp.float32)
    grad_q = (
        grad_q + jnp.einsum("hij,jhd->ihd", dscore_own, key_own, preferred_element_type=jnp.float32)
    ) * score_scale
    grad_k_own = (
        jnp.einsum("hij,ihd->jhd", dscore_own, query_block, preferred_element_type=jnp.float32)
        * score_scale
    )
    grad_v_own = jnp.einsum(
        "hij,ihd->jhd", prob_own_b, grad_block, preferred_element_type=jnp.float32
    )
    grad_k_prev = (
        jnp.einsum("hij,ihd->jhd", dscore_prev, query_block, preferred_element_type=jnp.float32)
        * score_scale
    )
    grad_v_prev = jnp.einsum(
        "hij,ihd->jhd", prob_prev_b, grad_block, preferred_element_type=jnp.float32
    )
    return grad_q, grad_k_own, grad_v_own, grad_k_prev, grad_v_prev


def halo_pairs(heads, cycle):
    pairs = []
    for h in range(heads):
        for c in range(cycle):
            src = h * cycle + c
            if h < heads // 2:
                if c + 1 < cycle:
                    pairs.append((src, src + 1))
                else:
                    pairs.append((src, (heads - 1 - h) * cycle + c))
            elif c > 0:
                pairs.append((src, src - 1))
    return pairs


def on_device(query_rows, key_rows, value_rows, grad_rows):
    heads = lax.axis_size("head")
    cycle = lax.axis_size(("ctx", "inner"))
    h = lax.axis_index("head")
    c = lax.axis_index(("ctx", "inner"))
    keep_low = (h == 1) | (h == 2)
    is_first = h % 2 == 0
    prev_valid = (h >= heads // 2) | (c > 0)
    partner = [(i, i ^ 1) for i in range(heads)]
    forward = halo_pairs(heads, cycle)
    backward = [(t, s) for s, t in forward]

    rows, all_heads, hd = query_rows.shape
    half = all_heads // 2
    hc = half // CHUNKS
    stacked = jnp.stack([query_rows, key_rows, value_rows, grad_rows])
    split = stacked.reshape(4, rows, 2, CHUNKS, hc, hd)
    keep = jnp.where(keep_low, split[:, :, 0], split[:, :, 1])
    send = jnp.where(keep_low, split[:, :, 1], split[:, :, 0])

    own_parts, back_parts = [], []
    for i in range(CHUNKS):
        own_i = keep[:, :, i]
        recv_i = lax.ppermute(send[:, :, i], "head", partner)
        first = jnp.where(is_first, own_i, recv_i)
        second = jnp.where(is_first, recv_i, own_i)
        blk = jnp.concatenate([first, second], axis=1)
        kv_prev = lax.ppermute(blk[1:3], ALL_AXES, forward)
        dq, dk_own, dv_own, dk_prev, dv_prev = block_side(
            blk[0], blk[3], kv_prev[0], kv_prev[1], blk[1], blk[2], prev_valid
        )
        dkv_next = lax.ppermute(
            jnp.stack([dk_prev, dv_prev]).astype(jnp.bfloat16), ALL_AXES, backward
        )
        dk = dk_own + dkv_next[0].astype(jnp.float32)
        dv = dv_own + dkv_next[1].astype(jnp.float32)
        grads = jnp.stack([dq, dk, dv]).astype(jnp.bfloat16)
        mine = jnp.where(is_first, grads[:, :rows], grads[:, rows:])
        theirs = jnp.where(is_first, grads[:, rows:], grads[:, :rows])
        own_parts.append(mine)
        back_parts.append(lax.ppermute(theirs, "head", partner))
    own_all = jnp.stack(own_parts, axis=2)
    back_all = jnp.stack(back_parts, axis=2)
    low = jnp.where(keep_low, own_all, back_all)
    high = jnp.where(keep_low, back_all, own_all)
    out = jnp.stack([low, high], axis=2).reshape(3, rows, all_heads, hd)
    return out[0], out[1], out[2]


def solution(mesh):
    spec = P(("head", "ctx", "inner"), None, None)
    return jax.shard_map(
        on_device, mesh=mesh, in_specs=(spec,) * 4, out_specs=(spec,) * 3, check_vma=False
    )
```

```python
import jax
import jax.numpy as jnp
from jax import lax
from jax.sharding import PartitionSpec as P

CHUNKS = 4
ALL_AXES = ("head", "ctx", "inner")


def tile_scores(query_block, key_block, score_scale):
    return (
        jnp.einsum("ihd,jhd->hij", query_block, key_block, preferred_element_type=jnp.float32)
        * score_scale
    )


def tile_sight(row_count, prev_valid):
    rows_iota = lax.broadcasted_iota(jnp.int32, (row_count, row_count), 0)
    cols_iota = lax.broadcasted_iota(jnp.int32, (row_count, row_count), 1)
    return ((cols_iota > rows_iota) & prev_valid, cols_iota <= rows_iota)


def block_side(query_block, grad_block, key_prev, value_prev, key_own, value_own, prev_valid):
    score_scale = query_block.shape[-1] ** (-0.5)
    sees_prev, sees_own = tile_sight(query_block.shape[0], prev_valid)
    scores_prev = tile_scores(query_block, key_prev, score_scale)
    scores_own = tile_scores(query_block, key_own, score_scale)
    row_top = jnp.maximum(
        jnp.max(jnp.where(sees_prev, scores_prev, -jnp.inf), axis=-1),
        jnp.max(jnp.where(sees_own, scores_own, -jnp.inf), axis=-1),
    )
    row_total = jnp.sum(
        jnp.where(sees_prev, jnp.exp(scores_prev - row_top[..., None]), 0.0), axis=-1
    )
    row_total = row_total + jnp.sum(
        jnp.where(sees_own, jnp.exp(scores_own - row_top[..., None]), 0.0), axis=-1
    )
    log_total = row_top + jnp.log(row_total)
    prob_prev = jnp.where(sees_prev, jnp.exp(scores_prev - log_total[..., None]), 0.0)
    prob_own = jnp.where(sees_own, jnp.exp(scores_own - log_total[..., None]), 0.0)
    prob_prev_b = prob_prev.astype(jnp.bfloat16)
    prob_own_b = prob_own.astype(jnp.bfloat16)
    attended = jnp.einsum(
        "hij,jhd->ihd", prob_prev_b, value_prev, preferred_element_type=jnp.float32
    )
    attended = attended + jnp.einsum(
        "hij,jhd->ihd", prob_own_b, value_own, preferred_element_type=jnp.float32
    )
    row_delta = jnp.sum(grad_block.astype(jnp.float32) * attended, axis=-1).T
    dprob_prev = jnp.einsum(
        "ihd,jhd->hij", grad_block, value_prev, preferred_element_type=jnp.float32
    )
    dprob_own = jnp.einsum(
        "ihd,jhd->hij", grad_block, value_own, preferred_element_type=jnp.float32
    )
    dscore_prev = (prob_prev * (dprob_prev - row_delta[..., None])).astype(jnp.bfloat16)
    dscore_own = (prob_own * (dprob_own - row_delta[..., None])).astype(jnp.bfloat16)
    grad_q = jnp.einsum("hij,jhd->ihd", dscore_prev, key_prev, preferred_element_type=jnp.float32)
    grad_q = (
        grad_q + jnp.einsum("hij,jhd->ihd", dscore_own, key_own, preferred_element_type=jnp.float32)
    ) * score_scale
    grad_k_own = (
        jnp.einsum("hij,ihd->jhd", dscore_own, query_block, preferred_element_type=jnp.float32)
        * score_scale
    )
    grad_v_own = jnp.einsum(
        "hij,ihd->jhd", prob_own_b, grad_block, preferred_element_type=jnp.float32
    )
    grad_k_prev = (
        jnp.einsum("hij,ihd->jhd", dscore_prev, query_block, preferred_element_type=jnp.float32)
        * score_scale
    )
    grad_v_prev = jnp.einsum(
        "hij,ihd->jhd", prob_prev_b, grad_block, preferred_element_type=jnp.float32
    )
    return grad_q, grad_k_own, grad_v_own, grad_k_prev, grad_v_prev


def halo_pairs(heads, cycle):
    pairs = []
    for h in range(heads):
        for c in range(cycle):
            src = h * cycle + c
            if h < heads // 2:
                if c + 1 < cycle:
                    pairs.append((src, src + 1))
                else:
                    pairs.append((src, (heads - 1 - h) * cycle + c))
            elif c > 0:
                pairs.append((src, src - 1))
    return pairs


def on_device(query_rows, key_rows, value_rows, grad_rows):
    heads = lax.axis_size("head")
    cycle = lax.axis_size(("ctx", "inner"))
    h = lax.axis_index("head")
    c = lax.axis_index(("ctx", "inner"))
    keep_low = (h == 1) | (h == 2)
    is_first = h % 2 == 0
    prev_valid = (h >= heads // 2) | (c > 0)
    partner = [(i, i ^ 1) for i in range(heads)]
    forward = halo_pairs(heads, cycle)
    backward = [(t, s) for s, t in forward]

    rows, all_heads, hd = query_rows.shape
    half = all_heads // 2
    hc = half // CHUNKS
    inputs = (query_rows, key_rows, value_rows, grad_rows)

    def chunk_of(low, i):
        lo = jnp.stack([a[:, i * hc : (i + 1) * hc] for a in inputs])
        hi = jnp.stack([a[:, half + i * hc : half + (i + 1) * hc] for a in inputs])
        return jnp.where(low, lo, hi)

    received = [
        lax.ppermute(chunk_of(jnp.logical_not(keep_low), i), "head", partner) for i in range(CHUNKS)
    ]
    own_parts, back_parts = [], []
    done = None
    for i in range(CHUNKS):
        own_i = chunk_of(keep_low, i)
        recv_i = received[i]
        first = jnp.where(is_first, own_i, recv_i)
        second = jnp.where(is_first, recv_i, own_i)
        blk = jnp.concatenate([first, second], axis=1)
        kv_prev = lax.ppermute(blk[1:3], ALL_AXES, forward)
        if done is not None:
            (blk, kv_prev), _ = lax.optimization_barrier(((blk, kv_prev), done))
        dq, dk_own, dv_own, dk_prev, dv_prev = block_side(
            blk[0], blk[3], kv_prev[0], kv_prev[1], blk[1], blk[2], prev_valid
        )
        dkv_prev = jnp.stack([dk_prev, dv_prev]).astype(jnp.bfloat16)
        done = (dq, dk_own, dv_own, dkv_prev)
        dkv_next = lax.ppermute(dkv_prev, ALL_AXES, backward)
        dk = dk_own + dkv_next[0].astype(jnp.float32)
        dv = dv_own + dkv_next[1].astype(jnp.float32)
        grads = jnp.stack([dq, dk, dv]).astype(jnp.bfloat16)
        mine = jnp.where(is_first, grads[:, :rows], grads[:, rows:])
        theirs = jnp.where(is_first, grads[:, rows:], grads[:, :rows])
        own_parts.append(mine)
        back_parts.append(lax.ppermute(theirs, "head", partner))
    own_all = jnp.concatenate(own_parts, axis=2)
    back_all = jnp.concatenate(back_parts, axis=2)
    outs = []
    for k in range(3):
        low = jnp.where(keep_low, own_all[k], back_all[k])
        high = jnp.where(keep_low, back_all[k], own_all[k])
        outs.append(jnp.concatenate([low, high], axis=1))
    return tuple(outs)


def solution(mesh):
    spec = P(("head", "ctx", "inner"), None, None)
    return jax.shard_map(
        on_device, mesh=mesh, in_specs=(spec,) * 4, out_specs=(spec,) * 3, check_vma=False
    )
```

```python
import jax
import jax.numpy as jnp
from jax import lax
from jax.sharding import PartitionSpec as P

CHUNKS = 4
GROUP = 2
ALL_AXES = ("head", "ctx", "inner")


def tile_scores(query_block, key_block, score_scale):
    return (
        jnp.einsum("ihd,jhd->hij", query_block, key_block, preferred_element_type=jnp.float32)
        * score_scale
    )


def tile_sight(row_count, prev_valid):
    rows_iota = lax.broadcasted_iota(jnp.int32, (row_count, row_count), 0)
    cols_iota = lax.broadcasted_iota(jnp.int32, (row_count, row_count), 1)
    return ((cols_iota > rows_iota) & prev_valid, cols_iota <= rows_iota)


def block_side(query_block, grad_block, key_prev, value_prev, key_own, value_own, prev_valid):
    score_scale = query_block.shape[-1] ** (-0.5)
    sees_prev, sees_own = tile_sight(query_block.shape[0], prev_valid)
    scores_prev = tile_scores(query_block, key_prev, score_scale)
    scores_own = tile_scores(query_block, key_own, score_scale)
    row_top = jnp.maximum(
        jnp.max(jnp.where(sees_prev, scores_prev, -jnp.inf), axis=-1),
        jnp.max(jnp.where(sees_own, scores_own, -jnp.inf), axis=-1),
    )
    row_total = jnp.sum(
        jnp.where(sees_prev, jnp.exp(scores_prev - row_top[..., None]), 0.0), axis=-1
    )
    row_total = row_total + jnp.sum(
        jnp.where(sees_own, jnp.exp(scores_own - row_top[..., None]), 0.0), axis=-1
    )
    log_total = row_top + jnp.log(row_total)
    prob_prev = jnp.where(sees_prev, jnp.exp(scores_prev - log_total[..., None]), 0.0)
    prob_own = jnp.where(sees_own, jnp.exp(scores_own - log_total[..., None]), 0.0)
    prob_prev_b = prob_prev.astype(jnp.bfloat16)
    prob_own_b = prob_own.astype(jnp.bfloat16)
    attended = jnp.einsum(
        "hij,jhd->ihd", prob_prev_b, value_prev, preferred_element_type=jnp.float32
    )
    attended = attended + jnp.einsum(
        "hij,jhd->ihd", prob_own_b, value_own, preferred_element_type=jnp.float32
    )
    row_delta = jnp.sum(grad_block.astype(jnp.float32) * attended, axis=-1).T
    dprob_prev = jnp.einsum(
        "ihd,jhd->hij", grad_block, value_prev, preferred_element_type=jnp.float32
    )
    dprob_own = jnp.einsum(
        "ihd,jhd->hij", grad_block, value_own, preferred_element_type=jnp.float32
    )
    dscore_prev = (prob_prev * (dprob_prev - row_delta[..., None])).astype(jnp.bfloat16)
    dscore_own = (prob_own * (dprob_own - row_delta[..., None])).astype(jnp.bfloat16)
    grad_q = jnp.einsum("hij,jhd->ihd", dscore_prev, key_prev, preferred_element_type=jnp.float32)
    grad_q = (
        grad_q + jnp.einsum("hij,jhd->ihd", dscore_own, key_own, preferred_element_type=jnp.float32)
    ) * score_scale
    grad_k_own = (
        jnp.einsum("hij,ihd->jhd", dscore_own, query_block, preferred_element_type=jnp.float32)
        * score_scale
    )
    grad_v_own = jnp.einsum(
        "hij,ihd->jhd", prob_own_b, grad_block, preferred_element_type=jnp.float32
    )
    grad_k_prev = (
        jnp.einsum("hij,ihd->jhd", dscore_prev, query_block, preferred_element_type=jnp.float32)
        * score_scale
    )
    grad_v_prev = jnp.einsum(
        "hij,ihd->jhd", prob_prev_b, grad_block, preferred_element_type=jnp.float32
    )
    return grad_q, grad_k_own, grad_v_own, grad_k_prev, grad_v_prev


def halo_pairs(heads, cycle):
    pairs = []
    for h in range(heads):
        for c in range(cycle):
            src = h * cycle + c
            if h < heads // 2:
                if c + 1 < cycle:
                    pairs.append((src, src + 1))
                else:
                    pairs.append((src, (heads - 1 - h) * cycle + c))
            elif c > 0:
                pairs.append((src, src - 1))
    return pairs


def on_device(query_rows, key_rows, value_rows, grad_rows):
    heads = lax.axis_size("head")
    cycle = lax.axis_size(("ctx", "inner"))
    h = lax.axis_index("head")
    c = lax.axis_index(("ctx", "inner"))
    keep_low = (h == 1) | (h == 2)
    is_first = h % 2 == 0
    prev_valid = (h >= heads // 2) | (c > 0)
    sender_first = is_first ^ ((h >= heads // 2) & (c == cycle - 1))
    partner = [(i, i ^ 1) for i in range(heads)]
    forward = halo_pairs(heads, cycle)
    backward = [(t, s) for s, t in forward]

    rows, all_heads, hd = query_rows.shape
    half = all_heads // 2
    hc = half // CHUNKS
    inputs = (query_rows, key_rows, value_rows, grad_rows)

    def chunk_of(arrays, low, i):
        lo = jnp.stack([a[:, i * hc : (i + 1) * hc] for a in arrays])
        hi = jnp.stack([a[:, half + i * hc : half + (i + 1) * hc] for a in arrays])
        return jnp.where(low, lo, hi)

    kv_kept = jnp.stack(
        [chunk_of((key_rows, value_rows), keep_low, i) for i in range(CHUNKS)]
    )
    kv_own_prev = lax.ppermute(kv_kept, ALL_AXES, forward)
    groups = [
        lax.ppermute(
            jnp.concatenate(
                [chunk_of(inputs, jnp.logical_not(keep_low), i) for i in range(g, g + GROUP)], axis=2
            ),
            "head",
            partner,
        )
        for g in range(0, CHUNKS, GROUP)
    ]
    own_parts, back_parts, returned = [], [], []
    forwarded = None
    for i in range(CHUNKS):
        own_i = chunk_of(inputs, keep_low, i)
        if i % GROUP == 0:
            recv_g = groups[i // GROUP]
            if i:
                recv_g, _ = lax.optimization_barrier((recv_g, own_parts[-1]))
            forwarded = lax.ppermute(recv_g[1:3], ALL_AXES, forward)
        j = i % GROUP
        recv_i = recv_g[:, :, j * hc : (j + 1) * hc]
        kv_other_prev = forwarded[:, :, j * hc : (j + 1) * hc]
        first = jnp.where(is_first, own_i, recv_i)
        second = jnp.where(is_first, recv_i, own_i)
        blk = jnp.concatenate([first, second], axis=1)
        kv_a = jnp.where(sender_first, kv_own_prev[i], kv_other_prev)
        kv_b = jnp.where(sender_first, kv_other_prev, kv_own_prev[i])
        kv_prev = jnp.concatenate([kv_a, kv_b], axis=1)
        waits = tuple(returned[-1:]) + tuple(back_parts[-2:-1])
        if waits:
            (blk, kv_prev), _ = lax.optimization_barrier(((blk, kv_prev), waits))
        dq, dk_own, dv_own, dk_prev, dv_prev = block_side(
            blk[0], blk[3], kv_prev[0], kv_prev[1], blk[1], blk[2], prev_valid
        )
        dkv_next = lax.ppermute(
            jnp.stack([dk_prev, dv_prev]).astype(jnp.bfloat16), ALL_AXES, backward
        )
        returned.append(dkv_next)
        dk = dk_own + dkv_next[0].astype(jnp.float32)
        dv = dv_own + dkv_next[1].astype(jnp.float32)
        grads = jnp.stack([dq, dk, dv]).astype(jnp.bfloat16)
        mine = jnp.where(is_first, grads[:, :rows], grads[:, rows:])
        theirs = jnp.where(is_first, grads[:, rows:], grads[:, :rows])
        own_parts.append(mine)
        back_parts.append(lax.ppermute(theirs, "head", partner))
    own_all = jnp.concatenate(own_parts, axis=2)
    back_all = jnp.concatenate(back_parts, axis=2)
    outs = []
    for k in range(3):
        low = jnp.where(keep_low, own_all[k], back_all[k])
        high = jnp.where(keep_low, back_all[k], own_all[k])
        outs.append(jnp.concatenate([low, high], axis=1))
    return tuple(outs)


def solution(mesh):
    spec = P(("head", "ctx", "inner"), None, None)
    return jax.shard_map(
        on_device, mesh=mesh, in_specs=(spec,) * 4, out_specs=(spec,) * 3, check_vma=False
    )
```

```python
import jax
import jax.numpy as jnp
from jax import lax
from jax.sharding import PartitionSpec as P

CHUNKS = 4
GROUP = 2
ALL_AXES = ("head", "ctx", "inner")


def block_side(query, grad, key_prev, value_prev, key_own, value_own, prev_valid):
    score_scale = query.shape[-1] ** (-0.5)
    rows = query.shape[1]
    rows_iota = lax.broadcasted_iota(jnp.int32, (rows, rows), 0)
    cols_iota = lax.broadcasted_iota(jnp.int32, (rows, rows), 1)
    sees_prev = (cols_iota > rows_iota) & prev_valid
    sees_own = cols_iota <= rows_iota

    def mm(spec, a, b):
        return jnp.einsum(spec, a, b, preferred_element_type=jnp.float32)

    scores_prev = mm("hid,hjd->hij", query, key_prev) * score_scale
    scores_own = mm("hid,hjd->hij", query, key_own) * score_scale
    row_top = jnp.maximum(
        jnp.max(jnp.where(sees_prev, scores_prev, -jnp.inf), axis=-1),
        jnp.max(jnp.where(sees_own, scores_own, -jnp.inf), axis=-1),
    )
    row_total = jnp.sum(
        jnp.where(sees_prev, jnp.exp(scores_prev - row_top[..., None]), 0.0), axis=-1
    )
    row_total = row_total + jnp.sum(
        jnp.where(sees_own, jnp.exp(scores_own - row_top[..., None]), 0.0), axis=-1
    )
    log_total = row_top + jnp.log(row_total)
    prob_prev = jnp.where(sees_prev, jnp.exp(scores_prev - log_total[..., None]), 0.0)
    prob_own = jnp.where(sees_own, jnp.exp(scores_own - log_total[..., None]), 0.0)
    prob_prev_b = prob_prev.astype(jnp.bfloat16)
    prob_own_b = prob_own.astype(jnp.bfloat16)
    attended = mm("hij,hjd->hid", prob_prev_b, value_prev) + mm("hij,hjd->hid", prob_own_b, value_own)
    row_delta = jnp.sum(grad.astype(jnp.float32) * attended, axis=-1)
    dprob_prev = mm("hid,hjd->hij", grad, value_prev)
    dprob_own = mm("hid,hjd->hij", grad, value_own)
    dscore_prev = (prob_prev * (dprob_prev - row_delta[..., None])).astype(jnp.bfloat16)
    dscore_own = (prob_own * (dprob_own - row_delta[..., None])).astype(jnp.bfloat16)
    grad_q = (mm("hij,hjd->hid", dscore_prev, key_prev) + mm("hij,hjd->hid", dscore_own, key_own)) * score_scale
    grad_k_own = mm("hij,hid->hjd", dscore_own, query) * score_scale
    grad_v_own = mm("hij,hid->hjd", prob_own_b, grad)
    grad_k_prev = mm("hij,hid->hjd", dscore_prev, query) * score_scale
    grad_v_prev = mm("hij,hid->hjd", prob_prev_b, grad)
    return grad_q, grad_k_own, grad_v_own, grad_k_prev, grad_v_prev


def halo_pairs(heads, cycle):
    pairs = []
    for h in range(heads):
        for c in range(cycle):
            src = h * cycle + c
            if h < heads // 2:
                if c + 1 < cycle:
                    pairs.append((src, src + 1))
                else:
                    pairs.append((src, (heads - 1 - h) * cycle + c))
            elif c > 0:
                pairs.append((src, src - 1))
    return pairs


def on_device(query_rows, key_rows, value_rows, grad_rows):
    heads = lax.axis_size("head")
    cycle = lax.axis_size(("ctx", "inner"))
    h = lax.axis_index("head")
    c = lax.axis_index(("ctx", "inner"))
    keep_low = (h == 1) | (h == 2)
    is_first = h % 2 == 0
    prev_valid = (h >= heads // 2) | (c > 0)
    sender_first = is_first ^ ((h >= heads // 2) & (c == cycle - 1))
    partner = [(i, i ^ 1) for i in range(heads)]
    forward = halo_pairs(heads, cycle)
    backward = [(t, s) for s, t in forward]

    rows, all_heads, hd = query_rows.shape
    half = all_heads // 2
    hc = half // CHUNKS
    inputs = tuple(jnp.transpose(a, (1, 0, 2)) for a in (query_rows, key_rows, value_rows, grad_rows))
    keep_at = jnp.where(keep_low, 0, half)
    send_at = half - keep_at

    def take(arrays, at, first_head, count):
        return jnp.stack([lax.dynamic_slice_in_dim(a, at + first_head, count, axis=0) for a in arrays])

    kv_own_prev = lax.ppermute(take(inputs[1:3], keep_at, 0, half), ALL_AXES, forward)
    groups = [
        lax.ppermute(take(inputs, send_at, g * hc, GROUP * hc), "head", partner)
        for g in range(0, CHUNKS, GROUP)
    ]
    own_parts, back_parts, returned = [], [], []
    for i in range(CHUNKS):
        own_i = take(inputs, keep_at, i * hc, hc)
        if i % GROUP == 0:
            recv_g = groups[i // GROUP]
            if i:
                recv_g, _ = lax.optimization_barrier((recv_g, own_parts[-1]))
            forwarded = lax.ppermute(recv_g[1:3], ALL_AXES, forward)
        j = (i % GROUP) * hc
        recv_i = recv_g[:, j : j + hc]
        kv_other_prev = forwarded[:, j : j + hc]
        kv_mine_prev = kv_own_prev[:, i * hc : (i + 1) * hc]
        first = jnp.where(is_first, own_i, recv_i)
        second = jnp.where(is_first, recv_i, own_i)
        blk = jnp.concatenate([first, second], axis=2)
        kv_a = jnp.where(sender_first, kv_mine_prev, kv_other_prev)
        kv_b = jnp.where(sender_first, kv_other_prev, kv_mine_prev)
        kv_prev = jnp.concatenate([kv_a, kv_b], axis=2)
        waits = tuple(returned[-1:]) + tuple(back_parts[-2:-1])
        if waits:
            (blk, kv_prev), _ = lax.optimization_barrier(((blk, kv_prev), waits))
        dq, dk_own, dv_own, dk_prev, dv_prev = block_side(
            blk[0], blk[3], kv_prev[0], kv_prev[1], blk[1], blk[2], prev_valid
        )
        dkv_next = lax.ppermute(
            jnp.stack([dk_prev, dv_prev]).astype(jnp.bfloat16), ALL_AXES, backward
        )
        returned.append(dkv_next)
        dk = dk_own + dkv_next[0].astype(jnp.float32)
        dv = dv_own + dkv_next[1].astype(jnp.float32)
        grads = jnp.stack([dq, dk, dv]).astype(jnp.bfloat16)
        mine = jnp.where(is_first, grads[:, :, :rows], grads[:, :, rows:])
        theirs = jnp.where(is_first, grads[:, :, rows:], grads[:, :, :rows])
        own_parts.append(mine)
        back_parts.append(lax.ppermute(theirs, "head", partner))
    own_all = jnp.concatenate(own_parts, axis=1)
    back_all = jnp.concatenate(back_parts, axis=1)
    low = jnp.where(keep_low, own_all, back_all)
    high = jnp.where(keep_low, back_all, own_all)
    out = jnp.concatenate([low, high], axis=1)
    return tuple(jnp.transpose(out[k], (1, 0, 2)) for k in range(3))


def solution(mesh):
    spec = P(("head", "ctx", "inner"), None, None)
    return jax.shard_map(
        on_device, mesh=mesh, in_specs=(spec,) * 4, out_specs=(spec,) * 3, check_vma=False
    )
```

```python
import jax
import jax.numpy as jnp
from jax import lax
from jax.sharding import PartitionSpec as P

CHUNKS = 4
GROUP = 2
RWAIT = False
RHOLD = False
ALL_AXES = ("head", "ctx", "inner")


def block_side(query, grad, key_prev, value_prev, key_own, value_own, prev_valid):
    score_scale = query.shape[-1] ** (-0.5)
    rows = query.shape[1]
    rows_iota = lax.broadcasted_iota(jnp.int32, (rows, rows), 0)
    cols_iota = lax.broadcasted_iota(jnp.int32, (rows, rows), 1)
    sees_prev = (cols_iota > rows_iota) & prev_valid
    sees_own = cols_iota <= rows_iota

    def mm(spec, a, b):
        return jnp.einsum(spec, a, b, preferred_element_type=jnp.float32)

    scores_prev = mm("hid,hjd->hij", query, key_prev) * score_scale
    scores_own = mm("hid,hjd->hij", query, key_own) * score_scale
    row_top = jnp.maximum(
        jnp.max(jnp.where(sees_prev, scores_prev, -jnp.inf), axis=-1),
        jnp.max(jnp.where(sees_own, scores_own, -jnp.inf), axis=-1),
    )
    row_total = jnp.sum(
        jnp.where(sees_prev, jnp.exp(scores_prev - row_top[..., None]), 0.0), axis=-1
    )
    row_total = row_total + jnp.sum(
        jnp.where(sees_own, jnp.exp(scores_own - row_top[..., None]), 0.0), axis=-1
    )
    log_total = row_top + jnp.log(row_total)
    prob_prev = jnp.where(sees_prev, jnp.exp(scores_prev - log_total[..., None]), 0.0)
    prob_own = jnp.where(sees_own, jnp.exp(scores_own - log_total[..., None]), 0.0)
    prob_prev_b = prob_prev.astype(jnp.bfloat16)
    prob_own_b = prob_own.astype(jnp.bfloat16)
    attended = mm("hij,hjd->hid", prob_prev_b, value_prev) + mm("hij,hjd->hid", prob_own_b, value_own)
    row_delta = jnp.sum(grad.astype(jnp.float32) * attended, axis=-1)
    dprob_prev = mm("hid,hjd->hij", grad, value_prev)
    dprob_own = mm("hid,hjd->hij", grad, value_own)
    dscore_prev = (prob_prev * (dprob_prev - row_delta[..., None])).astype(jnp.bfloat16)
    dscore_own = (prob_own * (dprob_own - row_delta[..., None])).astype(jnp.bfloat16)
    grad_q = (mm("hij,hjd->hid", dscore_prev, key_prev) + mm("hij,hjd->hid", dscore_own, key_own)) * score_scale
    grad_k_own = mm("hij,hid->hjd", dscore_own, query) * score_scale
    grad_v_own = mm("hij,hid->hjd", prob_own_b, grad)
    grad_k_prev = mm("hij,hid->hjd", dscore_prev, query) * score_scale
    grad_v_prev = mm("hij,hid->hjd", prob_prev_b, grad)
    return grad_q, grad_k_own, grad_v_own, grad_k_prev, grad_v_prev


def halo_pairs(heads, cycle):
    pairs = []
    for h in range(heads):
        for c in range(cycle):
            src = h * cycle + c
            if h < heads // 2:
                if c + 1 < cycle:
                    pairs.append((src, src + 1))
                else:
                    pairs.append((src, (heads - 1 - h) * cycle + c))
            elif c > 0:
                pairs.append((src, src - 1))
    return pairs


def on_device(query_rows, key_rows, value_rows, grad_rows):
    heads = lax.axis_size("head")
    cycle = lax.axis_size(("ctx", "inner"))
    h = lax.axis_index("head")
    c = lax.axis_index(("ctx", "inner"))
    keep_low = (h == 1) | (h == 2)
    is_first = h % 2 == 0
    prev_valid = (h >= heads // 2) | (c > 0)
    sender_first = is_first ^ ((h >= heads // 2) & (c == cycle - 1))
    partner = [(i, i ^ 1) for i in range(heads)]
    forward = halo_pairs(heads, cycle)
    backward = [(t, s) for s, t in forward]

    rows, all_heads, hd = query_rows.shape
    half = all_heads // 2
    hc = half // CHUNKS
    inputs = tuple(jnp.transpose(a, (1, 0, 2)) for a in (query_rows, key_rows, value_rows, grad_rows))
    keep_at = jnp.where(keep_low, 0, half)
    send_at = half - keep_at

    def take(arrays, at, first_head, count):
        return jnp.stack([lax.dynamic_slice_in_dim(a, at + first_head, count, axis=0) for a in arrays])

    kv_own_prev = lax.ppermute(take(inputs[1:3], keep_at, 0, half), ALL_AXES, forward)
    groups = [
        lax.ppermute(take(inputs, send_at, g * hc, GROUP * hc), "head", partner)
        for g in range(0, CHUNKS, GROUP)
    ]
    own_parts, back_parts, returned = [], [], []
    held = {}
    for i in range(CHUNKS):
        own_i = take(inputs, keep_at, i * hc, hc)
        if i % GROUP == 0:
            recv_g = held[i // GROUP] if i else groups[0]
            forwarded = lax.ppermute(recv_g[1:3], ALL_AXES, forward)
        j = (i % GROUP) * hc
        recv_i = recv_g[:, j : j + hc]
        kv_other_prev = forwarded[:, j : j + hc]
        kv_mine_prev = kv_own_prev[:, i * hc : (i + 1) * hc]
        first = jnp.where(is_first, own_i, recv_i)
        second = jnp.where(is_first, recv_i, own_i)
        blk = jnp.concatenate([first, second], axis=2)
        kv_a = jnp.where(sender_first, kv_mine_prev, kv_other_prev)
        kv_b = jnp.where(sender_first, kv_other_prev, kv_mine_prev)
        kv_prev = jnp.concatenate([kv_a, kv_b], axis=2)
        waits = tuple(returned[-1:]) + (tuple(back_parts[-2:-1]) if RWAIT else ())
        if waits:
            (blk, kv_prev), _ = lax.optimization_barrier(((blk, kv_prev), waits))
        dq, dk_own, dv_own, dk_prev, dv_prev = block_side(
            blk[0], blk[3], kv_prev[0], kv_prev[1], blk[1], blk[2], prev_valid
        )
        dkv_prev = jnp.stack([dk_prev, dv_prev]).astype(jnp.bfloat16)
        if (i + 1) % GROUP == 0 and i + 1 < CHUNKS:
            recv_next, dq, dkv_prev = lax.optimization_barrier((groups[(i + 1) // GROUP], dq, dkv_prev))
            held[(i + 1) // GROUP] = recv_next
        dkv_next = lax.ppermute(dkv_prev, ALL_AXES, backward)
        returned.append(dkv_next)
        dk = dk_own + dkv_next[0].astype(jnp.float32)
        dv = dv_own + dkv_next[1].astype(jnp.float32)
        grads = jnp.stack([dq, dk, dv]).astype(jnp.bfloat16)
        mine = jnp.where(is_first, grads[:, :, :rows], grads[:, :, rows:])
        theirs = jnp.where(is_first, grads[:, :, rows:], grads[:, :, :rows])
        if RHOLD and (i + 1) % GROUP == 0 and i + 1 < CHUNKS:
            theirs, _ = lax.optimization_barrier((theirs, held[(i + 1) // GROUP]))
        own_parts.append(mine)
        back_parts.append(lax.ppermute(theirs, "head", partner))
    own_all = jnp.concatenate(own_parts, axis=1)
    back_all = jnp.concatenate(back_parts, axis=1)
    low = jnp.where(keep_low, own_all, back_all)
    high = jnp.where(keep_low, back_all, own_all)
    out = jnp.concatenate([low, high], axis=1)
    return tuple(jnp.transpose(out[k], (1, 0, 2)) for k in range(3))


def solution(mesh):
    spec = P(("head", "ctx", "inner"), None, None)
    return jax.shard_map(
        on_device, mesh=mesh, in_specs=(spec,) * 4, out_specs=(spec,) * 3, check_vma=False
    )
```

```python
import jax
import jax.numpy as jnp
from jax import lax
from jax.sharding import PartitionSpec as P

SIZES = (6, 6, 6, 6)
GROUPS = (2, 2)
ALL_AXES = ("head", "ctx", "inner")


def block_side(query, grad, key_prev, value_prev, key_own, value_own, prev_valid):
    score_scale = query.shape[-1] ** (-0.5)
    rows = query.shape[1]
    rows_iota = lax.broadcasted_iota(jnp.int32, (rows, rows), 0)
    cols_iota = lax.broadcasted_iota(jnp.int32, (rows, rows), 1)
    sees_prev = (cols_iota > rows_iota) & prev_valid
    sees_own = cols_iota <= rows_iota

    def mm(spec, a, b):
        return jnp.einsum(spec, a, b, preferred_element_type=jnp.float32)

    scores_prev = mm("hid,hjd->hij", query, key_prev) * score_scale
    scores_own = mm("hid,hjd->hij", query, key_own) * score_scale
    row_top = jnp.maximum(
        jnp.max(jnp.where(sees_prev, scores_prev, -jnp.inf), axis=-1),
        jnp.max(jnp.where(sees_own, scores_own, -jnp.inf), axis=-1),
    )
    row_total = jnp.sum(
        jnp.where(sees_prev, jnp.exp(scores_prev - row_top[..., None]), 0.0), axis=-1
    )
    row_total = row_total + jnp.sum(
        jnp.where(sees_own, jnp.exp(scores_own - row_top[..., None]), 0.0), axis=-1
    )
    log_total = row_top + jnp.log(row_total)
    prob_prev = jnp.where(sees_prev, jnp.exp(scores_prev - log_total[..., None]), 0.0)
    prob_own = jnp.where(sees_own, jnp.exp(scores_own - log_total[..., None]), 0.0)
    prob_prev_b = prob_prev.astype(jnp.bfloat16)
    prob_own_b = prob_own.astype(jnp.bfloat16)
    attended = mm("hij,hjd->hid", prob_prev_b, value_prev) + mm("hij,hjd->hid", prob_own_b, value_own)
    row_delta = jnp.sum(grad.astype(jnp.float32) * attended, axis=-1)
    dprob_prev = mm("hid,hjd->hij", grad, value_prev)
    dprob_own = mm("hid,hjd->hij", grad, value_own)
    dscore_prev = (prob_prev * (dprob_prev - row_delta[..., None])).astype(jnp.bfloat16)
    dscore_own = (prob_own * (dprob_own - row_delta[..., None])).astype(jnp.bfloat16)
    grad_q = (mm("hij,hjd->hid", dscore_prev, key_prev) + mm("hij,hjd->hid", dscore_own, key_own)) * score_scale
    grad_k_own = mm("hij,hid->hjd", dscore_own, query) * score_scale
    grad_v_own = mm("hij,hid->hjd", prob_own_b, grad)
    grad_k_prev = mm("hij,hid->hjd", dscore_prev, query) * score_scale
    grad_v_prev = mm("hij,hid->hjd", prob_prev_b, grad)
    return grad_q, grad_k_own, grad_v_own, grad_k_prev, grad_v_prev


def halo_pairs(heads, cycle):
    pairs = []
    for h in range(heads):
        for c in range(cycle):
            src = h * cycle + c
            if h < heads // 2:
                if c + 1 < cycle:
                    pairs.append((src, src + 1))
                else:
                    pairs.append((src, (heads - 1 - h) * cycle + c))
            elif c > 0:
                pairs.append((src, src - 1))
    return pairs


def on_device(query_rows, key_rows, value_rows, grad_rows):
    heads = lax.axis_size("head")
    cycle = lax.axis_size(("ctx", "inner"))
    h = lax.axis_index("head")
    c = lax.axis_index(("ctx", "inner"))
    keep_low = (h == 1) | (h == 2)
    is_first = h % 2 == 0
    prev_valid = (h >= heads // 2) | (c > 0)
    sender_first = is_first ^ ((h >= heads // 2) & (c == cycle - 1))
    partner = [(i, i ^ 1) for i in range(heads)]
    forward = halo_pairs(heads, cycle)
    backward = [(t, s) for s, t in forward]

    rows, all_heads, hd = query_rows.shape
    half = all_heads // 2
    inputs = tuple(jnp.transpose(a, (1, 0, 2)) for a in (query_rows, key_rows, value_rows, grad_rows))
    keep_at = jnp.where(keep_low, 0, half)
    send_at = half - keep_at

    def take(arrays, at, first_head, count):
        return jnp.stack([lax.dynamic_slice_in_dim(a, at + first_head, count, axis=0) for a in arrays])

    offsets = [sum(SIZES[:i]) for i in range(len(SIZES) + 1)]
    starts = [sum(GROUPS[:g]) for g in range(len(GROUPS) + 1)]
    kv_own_prev = lax.ppermute(take(inputs[1:3], keep_at, 0, half), ALL_AXES, forward)
    group_kv, group_qg = [], []
    for g in range(len(GROUPS)):
        lo, count = offsets[starts[g]], offsets[starts[g + 1]] - offsets[starts[g]]
        group_kv.append(lax.ppermute(take(inputs[1:3], send_at, lo, count), "head", partner))
        group_qg.append(lax.ppermute(take(inputs[::3], send_at, lo, count), "head", partner))
    groups = [(kv, qg) for kv, qg in zip(group_kv, group_qg)]
    own_parts, back_parts, returned = [], [], []
    held = {0: groups[0]}
    g = -1
    for i, hc in enumerate(SIZES):
        at = offsets[i]
        own_i = take(inputs, keep_at, at, hc)
        if i in starts:
            g += 1
            recv_kv, recv_qg = held[g]
            forwarded = lax.ppermute(recv_kv, ALL_AXES, forward)
            recv_g = jnp.stack([recv_qg[0], recv_kv[0], recv_kv[1], recv_qg[1]])
        j = at - offsets[starts[g]]
        recv_i = recv_g[:, j : j + hc]
        kv_other_prev = forwarded[:, j : j + hc]
        kv_mine_prev = kv_own_prev[:, at : at + hc]
        first = jnp.where(is_first, own_i, recv_i)
        second = jnp.where(is_first, recv_i, own_i)
        blk = jnp.concatenate([first, second], axis=2)
        kv_a = jnp.where(sender_first, kv_mine_prev, kv_other_prev)
        kv_b = jnp.where(sender_first, kv_other_prev, kv_mine_prev)
        kv_prev = jnp.concatenate([kv_a, kv_b], axis=2)
        if returned:
            (blk, kv_prev), _ = lax.optimization_barrier(((blk, kv_prev), returned[-1]))
        dq, dk_own, dv_own, dk_prev, dv_prev = block_side(
            blk[0], blk[3], kv_prev[0], kv_prev[1], blk[1], blk[2], prev_valid
        )
        dkv_prev = jnp.stack([dk_prev, dv_prev]).astype(jnp.bfloat16)
        if i + 1 in starts[1:-1]:
            held[g + 1], dq, dkv_prev = lax.optimization_barrier((groups[g + 1], dq, dkv_prev))
        dkv_next = lax.ppermute(dkv_prev, ALL_AXES, backward)
        returned.append(dkv_next)
        dk = dk_own + dkv_next[0].astype(jnp.float32)
        dv = dv_own + dkv_next[1].astype(jnp.float32)
        grads = jnp.stack([dq, dk, dv]).astype(jnp.bfloat16)
        mine = jnp.where(is_first, grads[:, :, :rows], grads[:, :, rows:])
        theirs = jnp.where(is_first, grads[:, :, rows:], grads[:, :, :rows])
        own_parts.append(mine)
        back_parts.append(lax.ppermute(theirs, "head", partner))
    own_all = jnp.concatenate(own_parts, axis=1)
    back_all = jnp.concatenate(back_parts, axis=1)
    low = jnp.where(keep_low, own_all, back_all)
    high = jnp.where(keep_low, back_all, own_all)
    out = jnp.concatenate([low, high], axis=1)
    return tuple(jnp.transpose(out[k], (1, 0, 2)) for k in range(3))


def solution(mesh):
    spec = P(("head", "ctx", "inner"), None, None)
    return jax.shard_map(
        on_device, mesh=mesh, in_specs=(spec,) * 4, out_specs=(spec,) * 3, check_vma=False
    )
```

```python
import jax
import jax.numpy as jnp
from jax import lax
from jax.sharding import PartitionSpec as P

SIZES = (6, 6, 6, 6)
GROUPS = (2, 2)
ALL_AXES = ("head", "ctx", "inner")


def block_side(query, grad, key_prev, value_prev, key_own, value_own, prev_valid):
    score_scale = query.shape[-1] ** (-0.5)
    rows = query.shape[1]
    rows_iota = lax.broadcasted_iota(jnp.int32, (rows, rows), 0)
    cols_iota = lax.broadcasted_iota(jnp.int32, (rows, rows), 1)
    sees_prev = (cols_iota > rows_iota) & prev_valid
    sees_own = cols_iota <= rows_iota

    def mm(spec, a, b):
        return jnp.einsum(spec, a, b, preferred_element_type=jnp.float32)

    scores_prev = mm("hid,hjd->hij", query, key_prev) * score_scale
    scores_own = mm("hid,hjd->hij", query, key_own) * score_scale
    row_top = jnp.maximum(
        jnp.max(jnp.where(sees_prev, scores_prev, -jnp.inf), axis=-1),
        jnp.max(jnp.where(sees_own, scores_own, -jnp.inf), axis=-1),
    )
    row_total = jnp.sum(
        jnp.where(sees_prev, jnp.exp(scores_prev - row_top[..., None]), 0.0), axis=-1
    )
    row_total = row_total + jnp.sum(
        jnp.where(sees_own, jnp.exp(scores_own - row_top[..., None]), 0.0), axis=-1
    )
    log_total = row_top + jnp.log(row_total)
    prob_prev = jnp.where(sees_prev, jnp.exp(scores_prev - log_total[..., None]), 0.0)
    prob_own = jnp.where(sees_own, jnp.exp(scores_own - log_total[..., None]), 0.0)
    prob_prev_b = prob_prev.astype(jnp.bfloat16)
    prob_own_b = prob_own.astype(jnp.bfloat16)
    attended = mm("hij,hjd->hid", prob_prev_b, value_prev) + mm("hij,hjd->hid", prob_own_b, value_own)
    row_delta = jnp.sum(grad.astype(jnp.float32) * attended, axis=-1)
    dprob_prev = mm("hid,hjd->hij", grad, value_prev)
    dprob_own = mm("hid,hjd->hij", grad, value_own)
    dscore_prev = (prob_prev * (dprob_prev - row_delta[..., None])).astype(jnp.bfloat16)
    dscore_own = (prob_own * (dprob_own - row_delta[..., None])).astype(jnp.bfloat16)
    grad_q = (mm("hij,hjd->hid", dscore_prev, key_prev) + mm("hij,hjd->hid", dscore_own, key_own)) * score_scale
    grad_k_own = mm("hij,hid->hjd", dscore_own, query) * score_scale
    grad_v_own = mm("hij,hid->hjd", prob_own_b, grad)
    grad_k_prev = mm("hij,hid->hjd", dscore_prev, query) * score_scale
    grad_v_prev = mm("hij,hid->hjd", prob_prev_b, grad)
    return grad_q, grad_k_own, grad_v_own, grad_k_prev, grad_v_prev


def halo_pairs(heads, cycle):
    pairs = []
    for h in range(heads):
        for c in range(cycle):
            src = h * cycle + c
            if h < heads // 2:
                if c + 1 < cycle:
                    pairs.append((src, src + 1))
                else:
                    pairs.append((src, (heads - 1 - h) * cycle + c))
            elif c > 0:
                pairs.append((src, src - 1))
    return pairs


def on_device(query_rows, key_rows, value_rows, grad_rows):
    heads = lax.axis_size("head")
    cycle = lax.axis_size(("ctx", "inner"))
    h = lax.axis_index("head")
    c = lax.axis_index(("ctx", "inner"))
    keep_low = (h == 1) | (h == 2)
    is_first = h % 2 == 0
    prev_valid = (h >= heads // 2) | (c > 0)
    sender_first = is_first ^ ((h >= heads // 2) & (c == cycle - 1))
    partner = [(i, i ^ 1) for i in range(heads)]
    forward = halo_pairs(heads, cycle)
    backward = [(t, s) for s, t in forward]

    rows, all_heads, hd = query_rows.shape
    half = all_heads // 2
    inputs = tuple(jnp.transpose(a, (1, 0, 2)) for a in (query_rows, key_rows, value_rows, grad_rows))
    keep_at = jnp.where(keep_low, 0, half)
    send_at = half - keep_at

    def take(arrays, at, first_head, count):
        return jnp.stack([lax.dynamic_slice_in_dim(a, at + first_head, count, axis=0) for a in arrays])

    offsets = [sum(SIZES[:i]) for i in range(len(SIZES) + 1)]
    starts = [sum(GROUPS[:g]) for g in range(len(GROUPS) + 1)]
    kv_own_prev = lax.ppermute(take(inputs[1:3], keep_at, 0, half), ALL_AXES, forward)
    group_kv, group_qg = [], []
    for g in range(len(GROUPS)):
        lo, count = offsets[starts[g]], offsets[starts[g + 1]] - offsets[starts[g]]
        group_kv.append(lax.ppermute(take(inputs[1:3], send_at, lo, count), "head", partner))
        group_qg.append(lax.ppermute(take(inputs[::3], send_at, lo, count), "head", partner))
    groups = [(kv, qg) for kv, qg in zip(group_kv, group_qg)]
    own_parts, back_parts, returned = [], [], []
    held = {0: groups[0]}
    g = -1
    for i, hc in enumerate(SIZES):
        at = offsets[i]
        own_i = take(inputs, keep_at, at, hc)
        if i in starts:
            g += 1
            recv_kv, recv_qg = held[g]
            forwarded = lax.ppermute(recv_kv, ALL_AXES, forward)
            recv_g = jnp.stack([recv_qg[0], recv_kv[0], recv_kv[1], recv_qg[1]])
        j = at - offsets[starts[g]]
        recv_i = recv_g[:, j : j + hc]
        kv_other_prev = forwarded[:, j : j + hc]
        kv_mine_prev = kv_own_prev[:, at : at + hc]
        first = jnp.where(is_first, own_i, recv_i)
        second = jnp.where(is_first, recv_i, own_i)
        blk = jnp.concatenate([first, second], axis=2)
        kv_a = jnp.where(sender_first, kv_mine_prev, kv_other_prev)
        kv_b = jnp.where(sender_first, kv_other_prev, kv_mine_prev)
        kv_prev = jnp.concatenate([kv_a, kv_b], axis=2)
        if returned:
            (blk, kv_prev), _ = lax.optimization_barrier(((blk, kv_prev), returned[-1]))
        dq, dk_own, dv_own, dk_prev, dv_prev = block_side(
            blk[0], blk[3], kv_prev[0], kv_prev[1], blk[1], blk[2], prev_valid
        )
        dkv_prev = jnp.stack([dk_prev, dv_prev]).astype(jnp.bfloat16)
        if i + 1 in starts[1:-1]:
            held[g + 1], dq = lax.optimization_barrier((groups[g + 1], dq))
        dkv_next = lax.ppermute(dkv_prev, ALL_AXES, backward)
        returned.append(dkv_next)
        dk = dk_own + dkv_next[0].astype(jnp.float32)
        dv = dv_own + dkv_next[1].astype(jnp.float32)
        grads = jnp.stack([dq, dk, dv]).astype(jnp.bfloat16)
        mine = jnp.where(is_first, grads[:, :, :rows], grads[:, :, rows:])
        theirs = jnp.where(is_first, grads[:, :, rows:], grads[:, :, :rows])
        own_parts.append(mine)
        back_parts.append(lax.ppermute(theirs, "head", partner))
    own_all = jnp.concatenate(own_parts, axis=1)
    back_all = jnp.concatenate(back_parts, axis=1)
    low = jnp.where(keep_low, own_all, back_all)
    high = jnp.where(keep_low, back_all, own_all)
    out = jnp.concatenate([low, high], axis=1)
    return tuple(jnp.transpose(out[k], (1, 0, 2)) for k in range(3))


def solution(mesh):
    spec = P(("head", "ctx", "inner"), None, None)
    return jax.shard_map(
        on_device, mesh=mesh, in_specs=(spec,) * 4, out_specs=(spec,) * 3, check_vma=False
    )
```
